512 devices in a mesh: tm: 8 (over y), space: 64 (over x, z, core).
Axes of the slice: x: 4, y: 8, z: 8, core: 2. Of those that a mesh axis runs over, the one named last changes fastest.
Arguments:
- starts: float32 [8, 256, 32768], P('tm', None, 'space'), may hold values from -6 to 6
- vel_x: float32 [256, 32768], P(None, 'space'), may hold values from -1 to 1
- vel_y: float32 [256, 32768], P(None, 'space'), may hold values from -1 to 1
- kappa: float32 [256, 32768], P(None, 'space'), may hold values from 0.02 to 0.25
Outputs:
- new_ends: float32 [8, 256, 32768], P('tm', None, 'space')
The draws below stay inside these ranges and needn't reach their ends.
All inputs are finite; a program needn't handle non-finite values.
Results may differ from the reference program's by a relative error of at most 0.00002.
Values sent between devices are 32-bit elements; how exact they have to be, the bound alone decides.
No kernel may reach another device: no remote copies, remote signals or barrier semaphores. Data moves between devices by JAX's collectives and lax.ppermute only.
A program may use at most 64 MiB of HBM per device.

```python
import jax
import jax.numpy as jnp

ROWS = 256
FINE = 8
CSTEPS = 2
SLICES = 8
NC = 32768


def block_scale(rng, extent, pieces, low, high):
    def one(position, blocks):
        draws = jax.random.uniform(jax.random.fold_in(jax.random.fold_in(rng, 6), position), (blocks,), jnp.float32, low / len(pieces), high / len(pieces))
        return jnp.repeat(jnp.exp(draws), extent[position] // blocks).reshape((-1,) + (1,) * (len(extent) - position - 1))

    level = one(*pieces[0])
    for cut in pieces[1:]:
        level = level * one(*cut)
    return level


def gaussian(stream_key, extent, scale, most, shards=(), kind=jnp.bfloat16):
    values = scale * jax.random.normal(stream_key, extent, jnp.float32)
    if shards:
        values = values * block_scale(stream_key, extent, shards, -0.22, 0.18)
    return jnp.clip(values, -most, most).astype(kind)


def setup_inputs(seed: int = 0) -> dict:
    keys = jax.random.split(jax.random.key(seed), 5)
    starts = gaussian(keys[0], (SLICES, ROWS, NC), 1.0, 6.0, ((0, 8), (2, 64)), jnp.float32)
    vel_x = jnp.clip(jax.random.uniform(keys[1], (ROWS, NC), jnp.float32, -1.0, 1.0) * block_scale(keys[1], (ROWS, NC), ((1, 64),), -0.4, 0.0), -1.0, 1.0)
    vel_y = jnp.clip(jax.random.uniform(keys[2], (ROWS, NC), jnp.float32, -1.0, 1.0) * block_scale(keys[2], (ROWS, NC), ((1, 64),), -0.4, 0.0), -1.0, 1.0)
    kappa = jnp.clip(0.02 + 0.23 * jax.random.uniform(keys[3], (ROWS, NC), jnp.float32) ** block_scale(keys[3], (ROWS, NC), ((1, 64),), -0.2, 0.2), 0.02, 0.25)
    return dict(starts=starts, vel_x=vel_x, vel_y=vel_y, kappa=kappa)


DT = 1.0 / 12.0


def advance(field, vel_x, vel_y, kappa, size):
    padded = jnp.pad(field, 1)
    mid = padded[1:-1, 1:-1]
    left = padded[1:-1, :-2]
    right = padded[1:-1, 2:]
    upper = padded[:-2, 1:-1]
    lower = padded[2:, 1:-1]
    moved = jnp.maximum(vel_x, 0.0) * (mid - left) + jnp.minimum(vel_x, 0.0) * (right - mid)
    moved = moved + jnp.maximum(vel_y, 0.0) * (mid - upper) + jnp.minimum(vel_y, 0.0) * (lower - mid)
    spread = upper + lower + left + right - 4.0 * mid
    return mid - size * moved + size * kappa * spread


def coarse(field, vel_x, vel_y, kappa):
    for step in range(CSTEPS):
        field = advance(field, vel_x, vel_y, kappa, DT * FINE / CSTEPS)
    return field


def reference(starts, vel_x, vel_y, kappa):
    results = []
    previous = starts[0]
    for slot in range(SLICES):
        field = starts[slot]
        for step in range(FINE):
            field = advance(field, vel_x, vel_y, kappa, DT)
        if slot == 0:
            current = field
        else:
            current = coarse(previous, vel_x, vel_y, kappa) + (field - coarse(starts[slot], vel_x, vel_y, kappa))
        results.append(current)
        previous = current
    return jnp.stack(results)
```

```python
import jax
import jax.numpy as jnp
from jax import lax
from jax.sharding import PartitionSpec as P

FINE = 8
CSTEPS = 2


DT = 1.0 / 12.0


def shifted(block, axis, distance):
    devices = range(lax.axis_size(axis))
    route = [(i - distance, i) for i in devices if i - distance in devices]
    return lax.ppermute(block, axis, route)


def with_halo(cells, axis, width):
    head = cells[..., :width]
    tail = cells[..., cells.shape[-1] - width:]
    left = shifted(tail, axis, 1)
    right = shifted(head, axis, -1)
    return jnp.concatenate([left, cells, right], axis=-1)


def advance(wide, coef, size):
    padded = jnp.pad(wide, ((1, 1), (0, 0)))
    mid = padded[1:-1, 1:-1]
    left = padded[1:-1, :-2]
    right = padded[1:-1, 2:]
    upper = padded[:-2, 1:-1]
    lower = padded[2:, 1:-1]
    moved = jnp.maximum(coef[0], 0.0) * (mid - left) + jnp.minimum(coef[0], 0.0) * (right - mid)
    moved = (
        moved
        + jnp.maximum(coef[1], 0.0) * (mid - upper)
        + jnp.minimum(coef[1], 0.0) * (lower - mid)
    )
    spread = upper + lower + left + right - 4.0 * mid
    return mid - size * moved + size * coef[2] * spread


def local(starts, vel_x, vel_y, kappa):
    slices = lax.axis_size("tm")
    chain = CSTEPS * (slices - 1)
    top = FINE + chain
    n = starts.shape[-1]
    packed = jnp.stack([starts[0], vel_x, vel_y, kappa])
    wide = with_halo(packed, "space", top)
    state = wide[0]
    coef_all = wide[1:]

    def coef_at(h):
        return coef_all[:, :, top - h: top + n + h]

    def run(field, h, steps, size):
        for _ in range(steps):
            h -= 1
            field = advance(field, coef_at(h), size)
        return field, h

    field, h = run(state, top, FINE, DT)
    start_c = state[:, top - chain - CSTEPS: top + n + chain + CSTEPS]
    old_coarse, _ = run(start_c, chain + CSTEPS, CSTEPS, DT * FINE / CSTEPS)
    first = lax.axis_index("tm") == 0
    carried = jnp.where(first, field, field - old_coarse)
    current = carried
    h = chain
    for turn in range(slices - 1):
        incoming = shifted(current, "tm", 1)
        moved, h = run(incoming, h, CSTEPS, DT * FINE / CSTEPS)
        current = carried[:, chain - h: chain + n + h] + moved
    return current[None]


def solution(mesh):
    placed = (P("tm", None, "space"), P(None, "space"), P(None, "space"), P(None, "space"))
    return jax.shard_map(
        local, mesh=mesh, in_specs=placed, out_specs=P("tm", None, "space"), check_vma=False
    )
```

```python
import jax
import jax.numpy as jnp
from jax import lax
from jax.sharding import PartitionSpec as P

FINE = 8
CSTEPS = 2


DT = 1.0 / 12.0


def shifted(block, axis, distance):
    devices = range(lax.axis_size(axis))
    route = [(i - distance, i) for i in devices if i - distance in devices]
    return lax.ppermute(block, axis, route)


def with_halo(cells, axis, width):
    head = cells[..., :width]
    tail = cells[..., cells.shape[-1] - width:]
    left = shifted(tail, axis, 1)
    right = shifted(head, axis, -1)
    return jnp.concatenate([left, cells, right], axis=-1)


def advance(wide, coef, size):
    padded = jnp.pad(wide, ((1, 1), (0, 0)))
    mid = padded[1:-1, 1:-1]
    left = padded[1:-1, :-2]
    right = padded[1:-1, 2:]
    upper = padded[:-2, 1:-1]
    lower = padded[2:, 1:-1]
    moved = jnp.maximum(coef[0], 0.0) * (mid - left) + jnp.minimum(coef[0], 0.0) * (right - mid)
    moved = (
        moved
        + jnp.maximum(coef[1], 0.0) * (mid - upper)
        + jnp.minimum(coef[1], 0.0) * (lower - mid)
    )
    spread = upper + lower + left + right - 4.0 * mid
    return mid - size * moved + size * coef[2] * spread


def local(starts, vel_x, vel_y, kappa):
    slices = lax.axis_size("tm")
    chain = CSTEPS * (slices - 1)
    top = FINE + chain
    n = starts.shape[-1]
    packed = jnp.stack([starts[0], vel_x, vel_y, kappa])
    wide = with_halo(packed, "space", top)
    state = wide[0]
    coef_all = wide[1:]

    def coef_at(h):
        return coef_all[:, :, top - h: top + n + h]

    def run(field, h, steps, size):
        for _ in range(steps):
            h -= 1
            field = advance(field, coef_at(h), size)
        return field, h

    field, h = run(state, top, FINE, DT)
    start_c = state[:, top - chain - CSTEPS: top + n + chain + CSTEPS]
    old_coarse, _ = run(start_c, chain + CSTEPS, CSTEPS, DT * FINE / CSTEPS)
    me = lax.axis_index("tm")
    carried = jnp.where(me == 0, field, field - old_coarse)
    every = lax.all_gather(carried, "tm")

    def part(j, h):
        pos = j + me - (slices - 1)
        got = lax.dynamic_index_in_dim(every, jnp.maximum(pos, 0), 0, keepdims=False)
        got = got[:, chain - h: chain + n + h]
        return jnp.where(pos >= 0, got, jnp.zeros_like(got))

    h = chain
    current = part(0, h)
    for turn in range(1, slices):
        moved, h = run(current, h, CSTEPS, DT * FINE / CSTEPS)
        current = part(turn, h) + moved
    return current[None]


def solution(mesh):
    placed = (P("tm", None, "space"), P(None, "space"), P(None, "space"), P(None, "space"))
    return jax.shard_map(
        local, mesh=mesh, in_specs=placed, out_specs=P("tm", None, "space"), check_vma=False
    )
```

```python
import jax
import jax.numpy as jnp
from jax import lax
from jax.sharding import PartitionSpec as P

FINE = 8
CSTEPS = 2


DT = 1.0 / 12.0


def shifted(block, axis, distance):
    devices = range(lax.axis_size(axis))
    route = [(i - distance, i) for i in devices if i - distance in devices]
    return lax.ppermute(block, axis, route)


def with_halo(cells, axis, width):
    head = cells[..., :width]
    tail = cells[..., cells.shape[-1] - width:]
    left = shifted(tail, axis, 1)
    right = shifted(head, axis, -1)
    return jnp.concatenate([left, cells, right], axis=-1)


def advance(wide, coef, size):
    padded = jnp.pad(wide, ((1, 1), (0, 0)))
    mid = padded[1:-1, 1:-1]
    left = padded[1:-1, :-2]
    right = padded[1:-1, 2:]
    upper = padded[:-2, 1:-1]
    lower = padded[2:, 1:-1]
    moved = jnp.maximum(coef[0], 0.0) * (mid - left) + jnp.minimum(coef[0], 0.0) * (right - mid)
    moved = (
        moved
        + jnp.maximum(coef[1], 0.0) * (mid - upper)
        + jnp.minimum(coef[1], 0.0) * (lower - mid)
    )
    spread = upper + lower + left + right - 4.0 * mid
    return mid - size * moved + size * coef[2] * spread


def local(starts, vel_x, vel_y, kappa):
    slices = lax.axis_size("tm")
    chain = CSTEPS * (slices - 1)
    top = FINE + chain
    n = starts.shape[-1]
    packed = jnp.stack([starts[0], vel_x, vel_y, kappa])
    wide = with_halo(packed, "space", top)
    state = wide[0]
    coef_all = wide[1:]

    def coef_at(h):
        return coef_all[:, :, top - h: top + n + h]

    def run(field, h, steps, size):
        for _ in range(steps):
            h -= 1
            field = advance(field, coef_at(h), size)
        return field, h

    field, h = run(state, top, FINE, DT)
    start_c = state[:, top - chain - CSTEPS: top + n + chain + CSTEPS]
    old_coarse, _ = run(start_c, chain + CSTEPS, CSTEPS, DT * FINE / CSTEPS)
    me = lax.axis_index("tm")
    carried = jnp.where(me == 0, field, field - old_coarse)
    ring = [(i, (i + 1) % slices) for i in range(slices)]
    back = [((i + 1) % slices, i) for i in range(slices)]
    ahead = slices // 2
    behind = slices - 1 - ahead
    got = {slices - 1: carried}
    block = carried
    for r in range(1, ahead + 1):
        keep = chain - CSTEPS * (r - 1)
        block = lax.ppermute(block[:, chain - keep: chain + n + keep] if r == 1 else block, "tm", back)
        got[r - 1] = block
        if r < ahead:
            block = block[:, CSTEPS: block.shape[-1] - CSTEPS]
    wide_f = CSTEPS * behind
    block = carried[:, chain - wide_f: chain + n + wide_f]
    for r in range(1, behind + 1):
        block = lax.ppermute(block, "tm", ring)
        got[slices - 1 - r] = block

    def part(j, h):
        blk = got[j]
        extra = (blk.shape[-1] - n) // 2 - h
        blk = blk[:, extra: extra + n + 2 * h]
        return jnp.where(me >= slices - 1 - j, blk, jnp.zeros_like(blk))

    h = chain
    current = part(0, h)
    for turn in range(1, slices):
        moved, h = run(current, h, CSTEPS, DT * FINE / CSTEPS)
        current = part(turn, h) + moved
    return current[None]


def solution(mesh):
    placed = (P("tm", None, "space"), P(None, "space"), P(None, "space"), P(None, "space"))
    return jax.shard_map(
        local, mesh=mesh, in_specs=placed, out_specs=P("tm", None, "space"), check_vma=False
    )
```

```python
import jax
import jax.numpy as jnp
from jax import lax
from jax.sharding import PartitionSpec as P

FINE = 8
CSTEPS = 2


DT = 1.0 / 12.0


def shifted(block, axis, distance):
    devices = range(lax.axis_size(axis))
    route = [(i - distance, i) for i in devices if i - distance in devices]
    return lax.ppermute(block, axis, route)


def with_halo(cells, axis, width):
    head = cells[..., :width]
    tail = cells[..., cells.shape[-1] - width:]
    left = shifted(tail, axis, 1)
    right = shifted(head, axis, -1)
    return jnp.concatenate([left, cells, right], axis=-1)


def advance(wide, coef, size):
    padded = jnp.pad(wide, ((1, 1), (0, 0)))
    mid = padded[1:-1, 1:-1]
    left = padded[1:-1, :-2]
    right = padded[1:-1, 2:]
    upper = padded[:-2, 1:-1]
    lower = padded[2:, 1:-1]
    moved = jnp.maximum(coef[0], 0.0) * (mid - left) + jnp.minimum(coef[0], 0.0) * (right - mid)
    moved = (
        moved
        + jnp.maximum(coef[1], 0.0) * (mid - upper)
        + jnp.minimum(coef[1], 0.0) * (lower - mid)
    )
    spread = upper + lower + left + right - 4.0 * mid
    return mid - size * moved + size * coef[2] * spread


def local(starts, vel_x, vel_y, kappa):
    slices = lax.axis_size("tm")
    chain = CSTEPS * (slices - 1)
    top = FINE + chain
    n = starts.shape[-1]
    packed = jnp.stack([starts[0], vel_x, vel_y, kappa])
    wide = with_halo(packed, "space", top)
    state = wide[0]
    coef_all = wide[1:]

    def coef_at(h):
        return coef_all[:, :, top - h: top + n + h]

    def run(field, h, steps, size):
        for _ in range(steps):
            h -= 1
            field = advance(field, coef_at(h), size)
        return field, h

    field, h = run(state, top, FINE, DT)
    start_c = state[:, top - chain - CSTEPS: top + n + chain + CSTEPS]
    old_coarse, _ = run(start_c, chain + CSTEPS, CSTEPS, DT * FINE / CSTEPS)
    me = lax.axis_index("tm")
    carried = jnp.where(me == 0, field, field - old_coarse)
    ring = [(i, (i + 1) % slices) for i in range(slices)]
    back = [((i + 1) % slices, i) for i in range(slices)]
    ahead = slices // 2
    behind = slices - 1 - ahead
    rows = carried.shape[0]
    cuts = [(0, rows // 2), (rows // 2, rows)]
    pieces = {slices - 1: [carried]}
    wide_f = CSTEPS * behind
    bwd = [carried[a:b] for a, b in cuts]
    fwd = [carried[a:b, chain - wide_f: chain + n + wide_f] for a, b in cuts]
    for r in range(1, ahead + 1):
        keep = chain - CSTEPS * (r - 1)
        if r == 1:
            bwd = [blk[:, chain - keep: chain + n + keep] for blk in bwd]
        bwd = [lax.ppermute(blk, "tm", back) for blk in bwd]
        pieces[r - 1] = bwd
        if r < ahead:
            bwd = [blk[:, CSTEPS: blk.shape[-1] - CSTEPS] for blk in bwd]
        if r <= behind:
            fwd = [lax.ppermute(blk, "tm", ring) for blk in fwd]
            pieces[slices - 1 - r] = fwd
    got = {j: (p[0] if len(p) == 1 else jnp.concatenate(p, axis=0)) for j, p in pieces.items()}

    def part(j, h):
        blk = got[j]
        extra = (blk.shape[-1] - n) // 2 - h
        blk = blk[:, extra: extra + n + 2 * h]
        return jnp.where(me >= slices - 1 - j, blk, jnp.zeros_like(blk))

    h = chain
    current = part(0, h)
    for turn in range(1, slices):
        moved, h = run(current, h, CSTEPS, DT * FINE / CSTEPS)
        current = part(turn, h) + moved
    return current[None]


def solution(mesh):
    placed = (P("tm", None, "space"), P(None, "space"), P(None, "space"), P(None, "space"))
    return jax.shard_map(
        local, mesh=mesh, in_specs=placed, out_specs=P("tm", None, "space"), check_vma=False
    )
```

```python
import jax
import jax.numpy as jnp
from jax import lax
from jax.sharding import PartitionSpec as P

FINE = 8
CSTEPS = 2


DT = 1.0 / 12.0


def shifted(block, axis, distance):
    devices = range(lax.axis_size(axis))
    route = [(i - distance, i) for i in devices if i - distance in devices]
    return lax.ppermute(block, axis, route)


def with_halo(cells, axis, width):
    head = cells[..., :width]
    tail = cells[..., cells.shape[-1] - width:]
    left = shifted(tail, axis, 1)
    right = shifted(head, axis, -1)
    return jnp.concatenate([left, cells, right], axis=-1)


def advance(wide, coef, size):
    padded = jnp.pad(wide, ((1, 1), (0, 0)))
    mid = padded[1:-1, 1:-1]
    left = padded[1:-1, :-2]
    right = padded[1:-1, 2:]
    upper = padded[:-2, 1:-1]
    lower = padded[2:, 1:-1]
    moved = jnp.maximum(coef[0], 0.0) * (mid - left) + jnp.minimum(coef[0], 0.0) * (right - mid)
    moved = (
        moved
        + jnp.maximum(coef[1], 0.0) * (mid - upper)
        + jnp.minimum(coef[1], 0.0) * (lower - mid)
    )
    spread = upper + lower + left + right - 4.0 * mid
    return mid - size * moved + size * coef[2] * spread


def local(starts, vel_x, vel_y, kappa):
    slices = lax.axis_size("tm")
    chain = CSTEPS * (slices - 1)
    top = FINE + chain
    n = starts.shape[-1]
    packed = jnp.stack([starts[0], vel_x, vel_y, kappa])
    wide = with_halo(packed, "space", top)
    state = wide[0]
    coef_all = wide[1:]

    def coef_at(h):
        return coef_all[:, :, top - h: top + n + h]

    def run(field, h, steps, size):
        for _ in range(steps):
            h -= 1
            field = advance(field, coef_at(h), size)
        return field, h

    field, h = run(state, top, FINE, DT)
    start_c = state[:, top - chain - CSTEPS: top + n + chain + CSTEPS]
    old_coarse, _ = run(start_c, chain + CSTEPS, CSTEPS, DT * FINE / CSTEPS)
    me = lax.axis_index("tm")
    carried = jnp.where(me == 0, field, field - old_coarse)
    ring = [(i, i + 1) for i in range(slices - 1)]
    back = [((i + 1) % slices, i) for i in range(slices)]
    ahead = slices // 2
    behind = slices - 1 - ahead
    got = {slices - 1: carried}
    block = carried
    for r in range(1, ahead + 1):
        keep = chain - CSTEPS * (r - 1)
        block = lax.ppermute(block[:, chain - keep: chain + n + keep] if r == 1 else block, "tm", back)
        got[r - 1] = block
        if r < ahead:
            block = block[:, CSTEPS: block.shape[-1] - CSTEPS]
    wide_f = CSTEPS * behind
    block = carried[:, chain - wide_f: chain + n + wide_f]
    for r in range(1, behind + 1):
        block = lax.ppermute(block, "tm", ring)
        got[slices - 1 - r] = block

    def part(j, h):
        blk = got[j]
        extra = (blk.shape[-1] - n) // 2 - h
        blk = blk[:, extra: extra + n + 2 * h]
        if j >= ahead:
            return blk
        return jnp.where(me >= slices - 1 - j, blk, jnp.zeros_like(blk))

    h = chain
    current = part(0, h)
    for turn in range(1, slices):
        moved, h = run(current, h, CSTEPS, DT * FINE / CSTEPS)
        current = part(turn, h) + moved
    return current[None]


def solution(mesh):
    placed = (P("tm", None, "space"), P(None, "space"), P(None, "space"), P(None, "space"))
    return jax.shard_map(
        local, mesh=mesh, in_specs=placed, out_specs=P("tm", None, "space"), check_vma=False
    )
```

```python
import jax
import jax.numpy as jnp
from jax import lax
from jax.sharding import PartitionSpec as P

FINE = 8
CSTEPS = 2


DT = 1.0 / 12.0


def shifted(block, axis, distance):
    devices = range(lax.axis_size(axis))
    route = [(i - distance, i) for i in devices if i - distance in devices]
    return lax.ppermute(block, axis, route)


def with_halo(cells, axis, width):
    head = cells[..., :width]
    tail = cells[..., cells.shape[-1] - width:]
    left = shifted(tail, axis, 1)
    right = shifted(head, axis, -1)
    return jnp.concatenate([left, cells, right], axis=-1)


def advance(wide, coef, size):
    padded = jnp.pad(wide, ((1, 1), (0, 0)))
    mid = padded[1:-1, 1:-1]
    left = padded[1:-1, :-2]
    right = padded[1:-1, 2:]
    upper = padded[:-2, 1:-1]
    lower = padded[2:, 1:-1]
    moved = jnp.maximum(coef[0], 0.0) * (mid - left) + jnp.minimum(coef[0], 0.0) * (right - mid)
    moved = (
        moved
        + jnp.maximum(coef[1], 0.0) * (mid - upper)
        + jnp.minimum(coef[1], 0.0) * (lower - mid)
    )
    spread = upper + lower + left + right - 4.0 * mid
    return mid - size * moved + size * coef[2] * spread


def local(starts, vel_x, vel_y, kappa):
    slices = lax.axis_size("tm")
    chain = CSTEPS * (slices - 1)
    top = FINE + chain
    n = starts.shape[-1]
    packed = jnp.stack([starts[0], vel_x, vel_y, kappa])
    wide = with_halo(packed, "space", top)
    state = wide[0]
    coef_all = wide[1:]

    def coef_at(h):
        return coef_all[:, :, top - h: top + n + h]

    def run(field, h, steps, size):
        for _ in range(steps):
            h -= 1
            field = advance(field, coef_at(h), size)
        return field, h

    field, h = run(state, top, FINE, DT)
    start_c = state[:, top - chain - CSTEPS: top + n + chain + CSTEPS]
    old_coarse, _ = run(start_c, chain + CSTEPS, CSTEPS, DT * FINE / CSTEPS)
    me = lax.axis_index("tm")
    carried = jnp.where(me == 0, field, field - old_coarse)
    ring = [(i, i + 1) for i in range(slices - 1)]
    back = [((i + 1) % slices, i) for i in range(slices)]
    ahead = slices // 2
    behind = slices - 1 - ahead
    got = {slices - 1: carried}
    block = carried
    for r in range(1, ahead + 1):
        block = lax.ppermute(block, "tm", back)
        got[r - 1] = block
    wide_f = CSTEPS * behind
    block = carried[:, chain - wide_f: chain + n + wide_f]
    for r in range(1, behind + 1):
        block = lax.ppermute(block, "tm", ring)
        got[slices - 1 - r] = block

    def part(j, h):
        blk = got[j]
        extra = (blk.shape[-1] - n) // 2 - h
        blk = blk[:, extra: extra + n + 2 * h]
        if j >= ahead:
            return blk
        return jnp.where(me >= slices - 1 - j, blk, jnp.zeros_like(blk))

    h = chain
    current = part(0, h)
    for turn in range(1, slices):
        moved, h = run(current, h, CSTEPS, DT * FINE / CSTEPS)
        current = part(turn, h) + moved
    return current[None]


def solution(mesh):
    placed = (P("tm", None, "space"), P(None, "space"), P(None, "space"), P(None, "space"))
    return jax.shard_map(
        local, mesh=mesh, in_specs=placed, out_specs=P("tm", None, "space"), check_vma=False
    )
```

```python
import jax
import jax.numpy as jnp
from jax import lax
from jax.sharding import PartitionSpec as P

FINE = 8
CSTEPS = 2


DT = 1.0 / 12.0


def shifted(block, axis, distance):
    devices = range(lax.axis_size(axis))
    route = [(i - distance, i) for i in devices if i - distance in devices]
    return lax.ppermute(block, axis, route)


def with_halo(cells, axis, width):
    head = cells[..., :width]
    tail = cells[..., cells.shape[-1] - width:]
    left = shifted(tail, axis, 1)
    right = shifted(head, axis, -1)
    return jnp.concatenate([left, cells, right], axis=-1)


def advance(wide, coef, size):
    padded = jnp.pad(wide, ((1, 1), (0, 0)))
    mid = padded[1:-1, 1:-1]
    left = padded[1:-1, :-2]
    right = padded[1:-1, 2:]
    upper = padded[:-2, 1:-1]
    lower = padded[2:, 1:-1]
    moved = jnp.maximum(coef[0], 0.0) * (mid - left) + jnp.minimum(coef[0], 0.0) * (right - mid)
    moved = (
        moved
        + jnp.maximum(coef[1], 0.0) * (mid - upper)
        + jnp.minimum(coef[1], 0.0) * (lower - mid)
    )
    spread = upper + lower + left + right - 4.0 * mid
    return mid - size * moved + size * coef[2] * spread


def local(starts, vel_x, vel_y, kappa):
    slices = lax.axis_size("tm")
    chain = CSTEPS * (slices - 1)
    top = FINE + chain
    n = starts.shape[-1]
    packed = jnp.stack([starts[0], vel_x, vel_y, kappa])
    wide = with_halo(packed, "space", top)
    state = wide[0]
    coef_all = wide[1:]

    def coef_at(h):
        return coef_all[:, :, top - h: top + n + h]

    def run(field, h, steps, size):
        for _ in range(steps):
            h -= 1
            field = advance(field, coef_at(h), size)
        return field, h

    field, h = run(state, top, FINE, DT)
    start_c = state[:, top - chain - CSTEPS: top + n + chain + CSTEPS]
    old_coarse, _ = run(start_c, chain + CSTEPS, CSTEPS, DT * FINE / CSTEPS)
    me = lax.axis_index("tm")
    carried = jnp.where(me == 0, field, field - old_coarse)
    ring = [(i, i + 1) for i in range(slices - 1)]
    back = [((i + 1) % slices, i) for i in range(slices)]
    ahead = slices // 2
    behind = slices - 1 - ahead
    got = {slices - 1: carried}
    wide_f = CSTEPS * behind
    block = carried
    ahead_blk = carried[:, chain - wide_f: chain + n + wide_f]
    for r in range(1, ahead + 1):
        block = lax.ppermute(block, "tm", back)
        got[r - 1] = block
        if r <= behind:
            if r == behind:
                ahead_blk, got[r - 1] = lax.optimization_barrier((ahead_blk, block))
            ahead_blk = lax.ppermute(ahead_blk, "tm", ring)
            got[slices - 1 - r] = ahead_blk

    def part(j, h):
        blk = got[j]
        extra = (blk.shape[-1] - n) // 2 - h
        blk = blk[:, extra: extra + n + 2 * h]
        if j >= ahead:
            return blk
        return jnp.where(me >= slices - 1 - j, blk, jnp.zeros_like(blk))

    h = chain
    current = part(0, h)
    for turn in range(1, slices):
        moved, h = run(current, h, CSTEPS, DT * FINE / CSTEPS)
        current = part(turn, h) + moved
    return current[None]


def solution(mesh):
    placed = (P("tm", None, "space"), P(None, "space"), P(None, "space"), P(None, "space"))
    return jax.shard_map(
        local, mesh=mesh, in_specs=placed, out_specs=P("tm", None, "space"), check_vma=False
    )
```

```python
import jax
import jax.numpy as jnp
from jax import lax
from jax.sharding import PartitionSpec as P

FINE = 8
CSTEPS = 2


DT = 1.0 / 12.0


def shifted(block, axis, distance):
    devices = range(lax.axis_size(axis))
    route = [(i - distance, i) for i in devices if i - distance in devices]
    return lax.ppermute(block, axis, route)


def with_halo(cells, axis, width):
    head = cells[..., :width]
    tail = cells[..., cells.shape[-1] - width:]
    left = shifted(tail, axis, 1)
    right = shifted(head, axis, -1)
    return jnp.concatenate([left, cells, right], axis=-1)


def advance(wide, coef, size):
    padded = jnp.pad(wide, ((1, 1), (0, 0)))
    mid = padded[1:-1, 1:-1]
    left = padded[1:-1, :-2]
    right = padded[1:-1, 2:]
    upper = padded[:-2, 1:-1]
    lower = padded[2:, 1:-1]
    moved = jnp.maximum(coef[0], 0.0) * (mid - left) + jnp.minimum(coef[0], 0.0) * (right - mid)
    moved = (
        moved
        + jnp.maximum(coef[1], 0.0) * (mid - upper)
        + jnp.minimum(coef[1], 0.0) * (lower - mid)
    )
    spread = upper + lower + left + right - 4.0 * mid
    return mid - size * moved + size * coef[2] * spread


def local(starts, vel_x, vel_y, kappa):
    slices = lax.axis_size("tm")
    chain = CSTEPS * (slices - 1)
    top = FINE + chain
    n = starts.shape[-1]
    packed = jnp.stack([starts[0], vel_x, vel_y, kappa])
    wide = with_halo(packed, "space", top)
    state = wide[0]
    coef_all = wide[1:]

    def coef_at(h):
        return coef_all[:, :, top - h: top + n + h]

    def run(field, h, steps, size):
        for _ in range(steps):
            h -= 1
            field = advance(field, coef_at(h), size)
        return field, h

    field, h = run(state, top, FINE, DT)
    start_c = state[:, top - chain - CSTEPS: top + n + chain + CSTEPS]
    old_coarse, _ = run(start_c, chain + CSTEPS, CSTEPS, DT * FINE / CSTEPS)
    me = lax.axis_index("tm")
    carried = jnp.where(me == 0, field, field - old_coarse)
    ring = [(i, i + 1) for i in range(slices - 1)]
    back = [((i + 1) % slices, i) for i in range(slices)]
    ahead = slices // 2
    behind = slices - 1 - ahead
    got = {slices - 1: carried}
    wide_f = CSTEPS * ahead
    block = carried[:, chain - wide_f: chain + n + wide_f]
    late = carried
    for r in range(1, ahead + 1):
        block = lax.ppermute(block, "tm", ring)
        got[slices - 1 - r] = block
        if r <= behind:
            late = lax.ppermute(late, "tm", back)
            got[r - 1] = late

    def part(j, h):
        blk = got[j]
        extra = (blk.shape[-1] - n) // 2 - h
        blk = blk[:, extra: extra + n + 2 * h]
        if j >= behind:
            return blk
        return jnp.where(me >= slices - 1 - j, blk, jnp.zeros_like(blk))

    h = chain
    current = part(0, h)
    for turn in range(1, slices):
        moved, h = run(current, h, CSTEPS, DT * FINE / CSTEPS)
        current = part(turn, h) + moved
    return current[None]


def solution(mesh):
    placed = (P("tm", None, "space"), P(None, "space"), P(None, "space"), P(None, "space"))
    return jax.shard_map(
        local, mesh=mesh, in_specs=placed, out_specs=P("tm", None, "space"), check_vma=False
    )
```

```python
import jax
import jax.numpy as jnp
from jax import lax
from jax.sharding import PartitionSpec as P

FINE = 8
CSTEPS = 2


DT = 1.0 / 12.0


def shifted(block, axis, distance):
    devices = range(lax.axis_size(axis))
    route = [(i - distance, i) for i in devices if i - distance in devices]
    return lax.ppermute(block, axis, route)


def with_halo(cells, axis, width):
    head = cells[..., :width]
    tail = cells[..., cells.shape[-1] - width:]
    left = shifted(tail, axis, 1)
    right = shifted(head, axis, -1)
    return jnp.concatenate([left, cells, right], axis=-1)


def advance(wide, coef, size):
    padded = jnp.pad(wide, ((1, 1), (0, 0)))
    mid = padded[1:-1, 1:-1]
    left = padded[1:-1, :-2]
    right = padded[1:-1, 2:]
    upper = padded[:-2, 1:-1]
    lower = padded[2:, 1:-1]
    moved = jnp.maximum(coef[0], 0.0) * (mid - left) + jnp.minimum(coef[0], 0.0) * (right - mid)
    moved = (
        moved
        + jnp.maximum(coef[1], 0.0) * (mid - upper)
        + jnp.minimum(coef[1], 0.0) * (lower - mid)
    )
    spread = upper + lower + left + right - 4.0 * mid
    return mid - size * moved + size * coef[2] * spread


def local(starts, vel_x, vel_y, kappa):
    slices = lax.axis_size("tm")
    chain = CSTEPS * (slices - 1)
    top = FINE + chain
    n = starts.shape[-1]
    packed = jnp.stack([starts[0], vel_x, vel_y, kappa])
    wide = with_halo(packed, "space", top)
    state = wide[0]
    coef_all = wide[1:]

    def coef_at(h):
        return coef_all[:, :, top - h: top + n + h]

    def run(field, h, steps, size):
        for _ in range(steps):
            h -= 1
            field = advance(field, coef_at(h), size)
        return field, h

    field, h = run(state, top, FINE, DT)
    start_c = state[:, top - chain - CSTEPS: top + n + chain + CSTEPS]
    old_coarse, _ = run(start_c, chain + CSTEPS, CSTEPS, DT * FINE / CSTEPS)
    me = lax.axis_index("tm")
    carried = jnp.where(me == 0, field, field - old_coarse)
    ring = [(i, i + 1) for i in range(slices - 1)]
    back = [((i + 1) % slices, i) for i in range(slices)]
    ahead = slices // 2
    behind = slices - 1 - ahead
    got = {slices - 1: carried}
    wide_f = CSTEPS * behind
    near = CSTEPS * (ahead // 2)
    skip = [((i + 2) % slices, i) for i in range(slices)]
    block = carried
    ahead_blk = carried[:, chain - wide_f: chain + n + wide_f]
    for r in range(1, ahead):
        block = lax.ppermute(block, "tm", back)
        got[r - 1] = block
        if r == 2:
            far, fh = run(block, chain, CSTEPS * (ahead - near // CSTEPS), DT * FINE / CSTEPS)
            far = far[:, fh - near: fh + n + near]
        if r <= behind:
            if r == behind:
                ahead_blk, got[r - 1] = lax.optimization_barrier((ahead_blk, block))
            ahead_blk = lax.ppermute(ahead_blk, "tm", ring)
            got[slices - 1 - r] = ahead_blk
    far = lax.ppermute(far, "tm", skip)

    def part(j, h):
        blk = got[j]
        extra = (blk.shape[-1] - n) // 2 - h
        blk = blk[:, extra: extra + n + 2 * h]
        if j >= ahead:
            return blk
        return jnp.where(me >= slices - 1 - j, blk, jnp.zeros_like(blk))

    last = ahead - 1
    h = chain
    current = part(0, h)
    for turn in range(1, last):
        moved, h = run(current, h, CSTEPS, DT * FINE / CSTEPS)
        current = part(turn, h) + moved
    moved, h = run(current, h, CSTEPS, DT * FINE / CSTEPS)
    current = moved
    for turn in range(last + 1, slices):
        moved, h = run(current, h, CSTEPS, DT * FINE / CSTEPS)
        current = part(turn, h) + moved
    far = jnp.where(me >= slices - 1 - last, far, jnp.zeros_like(far))
    far, _ = run(far, near, near, DT * FINE / CSTEPS)
    current = current + far
    return current[None]


def solution(mesh):
    placed = (P("tm", None, "space"), P(None, "space"), P(None, "space"), P(None, "space"))
    return jax.shard_map(
        local, mesh=mesh, in_specs=placed, out_specs=P("tm", None, "space"), check_vma=False
    )
```

```python
import jax
import jax.numpy as jnp
from jax import lax
from jax.sharding import PartitionSpec as P

FINE = 8
CSTEPS = 2


DT = 1.0 / 12.0


def shifted(block, axis, distance):
    devices = range(lax.axis_size(axis))
    route = [(i - distance, i) for i in devices if i - distance in devices]
    return lax.ppermute(block, axis, route)


def with_halo(cells, axis, width):
    head = cells[..., :width]
    tail = cells[..., cells.shape[-1] - width:]
    left = shifted(tail, axis, 1)
    right = shifted(head, axis, -1)
    return jnp.concatenate([left, cells, right], axis=-1)


def advance(wide, coef, size):
    padded = jnp.pad(wide, ((1, 1), (0, 0)))
    mid = padded[1:-1, 1:-1]
    left = padded[1:-1, :-2]
    right = padded[1:-1, 2:]
    upper = padded[:-2, 1:-1]
    lower = padded[2:, 1:-1]
    moved = jnp.maximum(coef[0], 0.0) * (mid - left) + jnp.minimum(coef[0], 0.0) * (right - mid)
    moved = (
        moved
        + jnp.maximum(coef[1], 0.0) * (mid - upper)
        + jnp.minimum(coef[1], 0.0) * (lower - mid)
    )
    spread = upper + lower + left + right - 4.0 * mid
    return mid - size * moved + size * coef[2] * spread


def local(starts, vel_x, vel_y, kappa):
    slices = lax.axis_size("tm")
    chain = CSTEPS * (slices - 1)
    top = FINE + chain
    n = starts.shape[-1]
    packed = jnp.stack([starts[0], vel_x, vel_y, kappa])
    wide = with_halo(packed, "space", top)
    state = wide[0]
    coef_all = wide[1:]

    def coef_at(h):
        return coef_all[:, :, top - h: top + n + h]

    def run(field, h, steps, size):
        for _ in range(steps):
            h -= 1
            field = advance(field, coef_at(h), size)
        return field, h

    field, h = run(state, top, FINE, DT)
    start_c = state[:, top - chain - CSTEPS: top + n + chain + CSTEPS]
    old_coarse, _ = run(start_c, chain + CSTEPS, CSTEPS, DT * FINE / CSTEPS)
    me = lax.axis_index("tm")
    carried = jnp.where(me == 0, field, field - old_coarse)
    ring = [(i, i + 1) for i in range(slices - 1)]
    back = [((i + 1) % slices, i) for i in range(slices)]
    ahead = slices // 2
    behind = slices - 1 - ahead
    got = {slices - 1: carried}
    wide_f = CSTEPS * behind
    block = carried
    ahead_blk = carried[:, chain - wide_f: chain + n + wide_f]
    for r in range(1, ahead + 1):
        block = lax.ppermute(block, "tm", back)
        got[r - 1] = block
        if r < behind:
            ahead_blk = lax.ppermute(ahead_blk, "tm", ring)
            got[slices - 1 - r] = ahead_blk

    def part(j, h):
        blk = got[j]
        extra = (blk.shape[-1] - n) // 2 - h
        blk = blk[:, extra: extra + n + 2 * h]
        if j >= ahead:
            return blk
        return jnp.where(me >= slices - 1 - j, blk, jnp.zeros_like(blk))

    h = chain
    current = part(0, h)
    for turn in range(1, behind):
        moved, h = run(current, h, CSTEPS, DT * FINE / CSTEPS)
        current = part(turn, h) + moved
    ahead_blk, current = lax.optimization_barrier((ahead_blk, current))
    ahead_blk = lax.ppermute(ahead_blk, "tm", ring)
    got[slices - 1 - behind] = ahead_blk
    for turn in range(behind, slices):
        moved, h = run(current, h, CSTEPS, DT * FINE / CSTEPS)
        current = part(turn, h) + moved
    return current[None]


def solution(mesh):
    placed = (P("tm", None, "space"), P(None, "space"), P(None, "space"), P(None, "space"))
    return jax.shard_map(
        local, mesh=mesh, in_specs=placed, out_specs=P("tm", None, "space"), check_vma=False
    )
```

```python
import jax
import jax.numpy as jnp
from jax import lax
from jax.sharding import PartitionSpec as P

FINE = 8
CSTEPS = 2


DT = 1.0 / 12.0


def shifted(block, axis, distance):
    devices = range(lax.axis_size(axis))
    route = [(i - distance, i) for i in devices if i - distance in devices]
    return lax.ppermute(block, axis, route)


def with_halo(cells, axis, width):
    head = cells[..., :width]
    tail = cells[..., cells.shape[-1] - width:]
    left = shifted(tail, axis, 1)
    right = shifted(head, axis, -1)
    return jnp.concatenate([left, cells, right], axis=-1)


def advance(wide, coef, size):
    padded = jnp.pad(wide, ((1, 1), (0, 0)))
    mid = padded[1:-1, 1:-1]
    left = padded[1:-1, :-2]
    right = padded[1:-1, 2:]
    upper = padded[:-2, 1:-1]
    lower = padded[2:, 1:-1]
    moved = jnp.maximum(coef[0], 0.0) * (mid - left) + jnp.minimum(coef[0], 0.0) * (right - mid)
    moved = (
        moved
        + jnp.maximum(coef[1], 0.0) * (mid - upper)
        + jnp.minimum(coef[1], 0.0) * (lower - mid)
    )
    spread = upper + lower + left + right - 4.0 * mid
    return mid - size * moved + size * coef[2] * spread


def local(starts, vel_x, vel_y, kappa):
    slices = lax.axis_size("tm")
    chain = CSTEPS * (slices - 1)
    top = FINE + chain
    n = starts.shape[-1]
    packed = jnp.stack([starts[0], vel_x, vel_y, kappa])
    wide = with_halo(packed, "space", top)
    state = wide[0]
    coef_all = wide[1:]

    def coef_at(h):
        return coef_all[:, :, top - h: top + n + h]

    def run(field, h, steps, size):
        for _ in range(steps):
            h -= 1
            field = advance(field, coef_at(h), size)
        return field, h

    field, h = run(state, top, FINE, DT)
    start_c = state[:, top - chain - CSTEPS: top + n + chain + CSTEPS]
    old_coarse, _ = run(start_c, chain + CSTEPS, CSTEPS, DT * FINE / CSTEPS)
    me = lax.axis_index("tm")
    carried = jnp.where(me == 0, field, field - old_coarse)
    ring = [(i, i + 1) for i in range(slices - 1)]
    back = [((i + 1) % slices, i) for i in range(slices)]
    ahead = slices // 2
    behind = slices - 1 - ahead
    got = {slices - 1: carried}
    wide_f = CSTEPS * behind
    block = carried
    ahead_blk = carried[:, chain - wide_f: chain + n + wide_f]
    for r in range(1, ahead + 1):
        block = lax.ppermute(block, "tm", back)
        got[r - 1] = block
        if r < behind:
            ahead_blk = lax.ppermute(ahead_blk, "tm", ring)
            got[slices - 1 - r] = ahead_blk

    def part(j, h):
        blk = got[j]
        extra = (blk.shape[-1] - n) // 2 - h
        blk = blk[:, extra: extra + n + 2 * h]
        if j >= ahead:
            return blk
        return jnp.where(me >= slices - 1 - j, blk, jnp.zeros_like(blk))

    trimmed = lax.optimization_barrier(part(slices - 2, CSTEPS))
    h = chain
    current = part(0, h)
    for turn in range(1, behind):
        moved, h = run(current, h, CSTEPS, DT * FINE / CSTEPS)
        current = part(turn, h) + moved
    ahead_blk, current = lax.optimization_barrier((ahead_blk, current))
    ahead_blk = lax.ppermute(ahead_blk, "tm", ring)
    got[slices - 1 - behind] = ahead_blk
    for turn in range(behind, slices):
        moved, h = run(current, h, CSTEPS, DT * FINE / CSTEPS)
        current = (trimmed if turn == slices - 2 else part(turn, h)) + moved
    return current[None]


def solution(mesh):
    placed = (P("tm", None, "space"), P(None, "space"), P(None, "space"), P(None, "space"))
    return jax.shard_map(
        local, mesh=mesh, in_specs=placed, out_specs=P("tm", None, "space"), check_vma=False
    )
```

```python
import functools

import jax
import jax.numpy as jnp
from jax import lax
from jax.experimental import pallas as pl
from jax.experimental.pallas import tpu as pltpu
from jax.sharding import PartitionSpec as P

FINE = 8
CSTEPS = 2


DT = 1.0 / 12.0


def shifted(block, axis, distance):
    devices = range(lax.axis_size(axis))
    route = [(i - distance, i) for i in devices if i - distance in devices]
    return lax.ppermute(block, axis, route)


def with_halo(cells, axis, width):
    head = cells[..., :width]
    tail = cells[..., cells.shape[-1] - width:]
    left = shifted(tail, axis, 1)
    right = shifted(head, axis, -1)
    return jnp.concatenate([left, cells, right], axis=-1)


def advance(wide, coef, size):
    padded = jnp.pad(wide, ((1, 1), (0, 0)))
    mid = padded[1:-1, 1:-1]
    left = padded[1:-1, :-2]
    right = padded[1:-1, 2:]
    upper = padded[:-2, 1:-1]
    lower = padded[2:, 1:-1]
    moved = jnp.maximum(coef[0], 0.0) * (mid - left) + jnp.minimum(coef[0], 0.0) * (right - mid)
    moved = (
        moved
        + jnp.maximum(coef[1], 0.0) * (mid - upper)
        + jnp.minimum(coef[1], 0.0) * (lower - mid)
    )
    spread = upper + lower + left + right - 4.0 * mid
    return mid - size * moved + size * coef[2] * spread


def front_kernel(x_ref, o_ref, *, lead, keep):
    c = x_ref[0]
    vx = x_ref[1]
    vy = x_ref[2]
    ka = x_ref[3]
    axp = jnp.maximum(vx, 0.0)
    axm = jnp.minimum(vx, 0.0)
    ayp = jnp.maximum(vy, 0.0)
    aym = jnp.minimum(vy, 0.0)
    lane = lax.broadcasted_iota(jnp.int32, c.shape, 1)
    width = c.shape[0]
    rows = c.shape[1]

    def step(mid, size):
        left = pltpu.roll(mid, 1, 0)
        right = pltpu.roll(mid, width - 1, 0)
        upper = jnp.where(lane == 0, 0.0, pltpu.roll(mid, 1, 1))
        lower = jnp.where(lane == rows - 1, 0.0, pltpu.roll(mid, rows - 1, 1))
        moved = axp * (mid - left) + axm * (right - mid)
        moved = moved + ayp * (mid - upper) + aym * (lower - mid)
        spread = upper + lower + left + right - 4.0 * mid
        return mid - size * moved + size * ka * spread

    field = c
    for _ in range(FINE):
        field = step(field, DT)
    coarse_end = c
    for _ in range(CSTEPS):
        coarse_end = step(coarse_end, DT * FINE / CSTEPS)
    first = lax.axis_index("tm") == 0
    out = jnp.where(first, field, field - coarse_end)
    o_ref[...] = out[lead: lead + keep]


def local(starts, vel_x, vel_y, kappa):
    slices = lax.axis_size("tm")
    chain = CSTEPS * (slices - 1)
    lead = 8
    top = FINE + chain + 2
    n = starts.shape[-1]
    packed = jnp.stack([starts[0], vel_x, vel_y, kappa])
    wide = with_halo(packed, "space", top)
    state = wide[0]
    coef_all = wide[1:]

    def coef_at(h):
        return coef_all[:, :, top - h: top + n + h]

    def run(field, h, steps, size):
        for _ in range(steps):
            h -= 1
            field = advance(field, coef_at(h), size)
        return field, h

    me = lax.axis_index("tm")
    keep = n + 2 * (top - lead)
    cols_first = jnp.swapaxes(wide, 1, 2)
    out = pl.pallas_call(
        functools.partial(front_kernel, lead=lead, keep=keep),
        out_shape=jax.ShapeDtypeStruct((keep, cols_first.shape[-1]), jnp.float32),
    )(cols_first)
    carried = jnp.swapaxes(out, 0, 1)
    have = top - lead
    ring = [(i, i + 1) for i in range(slices - 1)]
    back = [((i + 1) % slices, i) for i in range(slices)]
    ahead = slices // 2
    behind = slices - 1 - ahead
    got = {slices - 1: carried}
    wide_f = CSTEPS * behind
    block = carried
    ahead_blk = carried[:, have - wide_f: have + n + wide_f]
    for r in range(1, ahead + 1):
        block = lax.ppermute(block, "tm", back)
        got[r - 1] = block
        if r < behind:
            ahead_blk = lax.ppermute(ahead_blk, "tm", ring)
            got[slices - 1 - r] = ahead_blk

    def part(j, h):
        blk = got[j]
        extra = (blk.shape[-1] - n) // 2 - h
        blk = blk[:, extra: extra + n + 2 * h]
        if j >= ahead:
            return blk
        return jnp.where(me >= slices - 1 - j, blk, jnp.zeros_like(blk))

    trimmed = lax.optimization_barrier(part(slices - 2, CSTEPS))
    h = chain
    current = part(0, h)
    for turn in range(1, behind):
        moved, h = run(current, h, CSTEPS, DT * FINE / CSTEPS)
        current = part(turn, h) + moved
    ahead_blk, current = lax.optimization_barrier((ahead_blk, current))
    ahead_blk = lax.ppermute(ahead_blk, "tm", ring)
    got[slices - 1 - behind] = ahead_blk
    for turn in range(behind, slices):
        moved, h = run(current, h, CSTEPS, DT * FINE / CSTEPS)
        current = (trimmed if turn == slices - 2 else part(turn, h)) + moved
    return current[None]


def solution(mesh):
    placed = (P("tm", None, "space"), P(None, "space"), P(None, "space"), P(None, "space"))
    return jax.shard_map(
        local, mesh=mesh, in_specs=placed, out_specs=P("tm", None, "space"), check_vma=False
    )
```

```python
import jax
import jax.numpy as jnp
from jax import lax
from jax.sharding import PartitionSpec as P

FINE = 8
CSTEPS = 2


DT = 1.0 / 12.0


def shifted(block, axis, distance):
    devices = range(lax.axis_size(axis))
    route = [(i - distance, i) for i in devices if i - distance in devices]
    return lax.ppermute(block, axis, route)


def with_halo(cells, axis, width):
    head = cells[..., :width]
    tail = cells[..., cells.shape[-1] - width:]
    left = shifted(tail, axis, 1)
    right = shifted(head, axis, -1)
    return jnp.concatenate([left, cells, right], axis=-1)


def advance(wide, coef, size):
    padded = jnp.pad(wide, ((1, 1), (0, 0)))
    mid = padded[1:-1, 1:-1]
    left = padded[1:-1, :-2]
    right = padded[1:-1, 2:]
    upper = padded[:-2, 1:-1]
    lower = padded[2:, 1:-1]
    moved = jnp.maximum(coef[0], 0.0) * (mid - left) + jnp.minimum(coef[0], 0.0) * (right - mid)
    moved = (
        moved
        + jnp.maximum(coef[1], 0.0) * (mid - upper)
        + jnp.minimum(coef[1], 0.0) * (lower - mid)
    )
    spread = upper + lower + left + right - 4.0 * mid
    return mid - size * moved + size * coef[2] * spread


def local(starts, vel_x, vel_y, kappa):
    slices = lax.axis_size("tm")
    chain = CSTEPS * (slices - 1)
    top = FINE + chain
    n = starts.shape[-1]
    packed = jnp.stack([starts[0], vel_x, vel_y, kappa])
    wide = with_halo(packed, "space", top)
    state = wide[0]
    coef_all = wide[1:]

    def coef_at(h):
        return coef_all[:, :, top - h: top + n + h]

    def run(field, h, steps, size):
        for _ in range(steps):
            h -= 1
            field = advance(field, coef_at(h), size)
        return field, h

    field, h = run(state, top, FINE, DT)
    start_c = state[:, top - chain - CSTEPS: top + n + chain + CSTEPS]
    old_coarse, _ = run(start_c, chain + CSTEPS, CSTEPS, DT * FINE / CSTEPS)
    me = lax.axis_index("tm")
    carried = jnp.where(me == 0, field, field - old_coarse)
    ring = [(i, i + 1) for i in range(slices - 1)]
    back = [((i + 1) % slices, i) for i in range(slices)]
    ahead = slices // 2
    behind = slices - 1 - ahead
    got = {slices - 1: carried}
    wide_f = CSTEPS * behind
    block = carried
    ahead_blk = carried[:, chain - wide_f: chain + n + wide_f]
    for r in range(1, ahead + 1):
        block = lax.ppermute(block, "tm", back)
        got[r - 1] = block
        if r < behind:
            ahead_blk = lax.ppermute(ahead_blk, "tm", ring)
            got[slices - 1 - r] = ahead_blk

    def part(j, h):
        blk = got[j]
        extra = (blk.shape[-1] - n) // 2 - h
        blk = blk[:, extra: extra + n + 2 * h]
        if j >= ahead:
            return blk
        return jnp.where(me >= slices - 1 - j, blk, jnp.zeros_like(blk))

    trimmed, own = lax.optimization_barrier((part(slices - 2, CSTEPS), part(slices - 1, 0)))
    h = chain
    current = part(0, h)
    for turn in range(1, behind):
        moved, h = run(current, h, CSTEPS, DT * FINE / CSTEPS)
        current = part(turn, h) + moved
    ahead_blk, current = lax.optimization_barrier((ahead_blk, current))
    ahead_blk = lax.ppermute(ahead_blk, "tm", ring)
    got[slices - 1 - behind] = ahead_blk
    for turn in range(behind, slices):
        moved, h = run(current, h, CSTEPS, DT * FINE / CSTEPS)
        current = {slices - 2: trimmed, slices - 1: own}.get(turn, None)
        current = (part(turn, h) if current is None else current) + moved
    return current[None]


def solution(mesh):
    placed = (P("tm", None, "space"), P(None, "space"), P(None, "space"), P(None, "space"))
    return jax.shard_map(
        local, mesh=mesh, in_specs=placed, out_specs=P("tm", None, "space"), check_vma=False
    )
```
